32 devices in a mesh: groups: 2 (over x), tm: 8 (over z, y), dp: 2 (over core).
Axes of the slice: x: 2, y: 2, z: 4, core: 2. Of those that a mesh axis runs over, the one named last changes fastest.
Arguments:
- clips: bfloat16 [4, 16, 32, 16, 256], P(('groups', 'dp'), 'tm'), parts along dimension 0, may hold values from -6 to 6
- kernel: bfloat16 [3, 3, 3, 256, 256], replicated, may hold values from -0.078125 to 0.078125
- cotangent: bfloat16 [4, 16, 32, 16, 256], P(('groups', 'dp'), 'tm'), parts along dimension 0, may hold values from -6 to 6
Outputs:
- output: bfloat16 [4, 16, 32, 16, 256], P(('groups', 'dp'), 'tm'), parts along dimension 0
- grad_input: bfloat16 [4, 16, 32, 16, 256], P(('groups', 'dp'), 'tm'), parts along dimension 0
- grad_kernel: float32 [6, 3, 3, 256, 256], P('groups', None, None, ('tm', 'dp')), parts along dimension 0
The draws below stay inside these ranges and needn't reach their ends.
There are 2 independent parts, one for each index of `groups`. The reference program is written for one: setup_inputs(seed, part) draws one part's arguments, and reference() takes and returns one part's arrays. A program takes and returns all parts, laid end to end along the dimension named above; an argument that names none is the same for every part. Nothing has to cross between parts.
All inputs are finite; a program needn't handle non-finite values.
Results may differ from the reference program's by a relative error of at most 0.004.
Values may be sent and summed in bfloat16 or wider, within the bound.
No kernel may reach another device: no remote copies, remote signals or barrier semaphores. Data moves between devices by JAX's collectives and lax.ppermute only.
A program may use at most 128 MiB of HBM per device.

```python
import jax
import jax.numpy as jnp
from jax import lax

C = 256
H = 32
W = 16
CLIPS = 2
FRAMES = 16


def spiked(values, rng, source, target, parts, factor):
    def block_of(axis_at):
        return (jnp.arange(values.shape[axis_at]) // (values.shape[axis_at] // parts)).reshape((-1,) + (1,) * (values.ndim - 1 - axis_at))

    one_side = jax.random.permutation(rng, parts)[block_of(target)]
    far = (block_of(target) + parts // 2) % parts
    return jnp.where((block_of(source) == one_side) | (block_of(source) == far), factor * values, values)


def levels(rng, extent, split, smallest, top_value):
    def one(position, blocks):
        steps = jax.random.uniform(jax.random.fold_in(jax.random.fold_in(rng, 6), position), (blocks,), jnp.float32, smallest / len(split), top_value / len(split))
        return jnp.repeat(jnp.exp(steps), extent[position] // blocks).reshape((-1,) + (1,) * (len(extent) - position - 1))

    factor_of = one(*split[0])
    for cut in split[1:]:
        factor_of = factor_of * one(*cut)
    return factor_of


def noise(key, dims, scale, bound, cuts=(), kind=jnp.bfloat16):
    entries = scale * jax.random.normal(key, dims, jnp.float32)
    if cuts:
        entries = entries * levels(key, dims, cuts, -0.22, 0.18)
    return jnp.clip(entries, -bound, bound).astype(kind)


def gaussian_with(key, dims, deviation, most, shards, heavy, held_as=jnp.bfloat16):
    values = deviation * jax.random.normal(key, dims, jnp.float32)
    if shards:
        values = values * levels(key, dims, shards, -0.22, 0.18)
    return jnp.clip(spiked(values, jax.random.fold_in(key, 3), *heavy), -most, most).astype(held_as)


def setup_inputs(seed: int = 0, part: int = 0) -> dict:
    seeds = jax.random.split(jax.random.key(seed), 4)
    own_keys = jax.random.split(jax.random.fold_in(seeds[3], part), 4)
    clips = gaussian_with(own_keys[0], (CLIPS, FRAMES, H, W, C), 1.0, 6.0, ((0, 2), (1, 8)), (1, 4, 8, 2.0))
    kernel = noise(seeds[1], (3, 3, 3, C, C), (27 * C) ** -0.5, 0.078125)
    cotangent = noise(own_keys[2], (CLIPS, FRAMES, H, W, C), 1.0, 6.0, ((0, 2), (1, 8)))
    return dict(clips=clips, kernel=kernel, cotangent=cotangent)


def convolve(source, kernel, time_pad, flipped):
    if flipped:
        kernel = lax.rev(kernel, (0, 1, 2))
        layout = "DHWOI"
    else:
        layout = "DHWIO"
    return lax.conv_general_dilated(source, kernel, (1, 1, 1), [time_pad, (1, 1), (1, 1)], dimension_numbers=("NDHWC", layout, "NDHWC"), preferred_element_type=jnp.float32)


def kernel_terms(extended, cotangent):
    frames = cotangent.shape[1]
    height = cotangent.shape[2]
    width = cotangent.shape[3]
    chans = cotangent.shape[4]
    spaced = jnp.pad(extended, ((0, 0), (0, 0), (1, 1), (1, 1), (0, 0)))
    flat_grad = cotangent.reshape(-1, chans)
    pieces = []
    for kt in range(3):
        for kh in range(3):
            for kw in range(3):
                window = spaced[:, kt:kt + frames, kh:kh + height, kw:kw + width, :].reshape(-1, chans)
                pieces.append(lax.dot_general(window, flat_grad, (((0,), (0,)), ((), ())), preferred_element_type=jnp.float32))
    return jnp.stack(pieces).reshape(3, 3, 3, chans, chans)


def reference(clips, kernel, cotangent):
    wide = clips.astype(jnp.float32)
    act = jax.nn.silu(wide).astype(jnp.bfloat16)
    extended = jnp.pad(act, ((0, 0), (2, 0), (0, 0), (0, 0), (0, 0)))
    conv = convolve(extended, kernel, (0, 0), False)
    output = (wide + conv).astype(jnp.bfloat16)
    later = jnp.pad(cotangent, ((0, 0), (0, 2), (0, 0), (0, 0), (0, 0)))
    grad_act = convolve(later, kernel, (0, 0), True)
    sig = jax.nn.sigmoid(wide)
    grad_input = (cotangent.astype(jnp.float32) + grad_act * sig * (1.0 + wide * (1.0 - sig))).astype(jnp.bfloat16)
    grad_kernel = kernel_terms(extended, cotangent)
    return output, grad_input, grad_kernel
```

```python
import jax
import jax.numpy as jnp
from jax import lax
from jax.sharding import PartitionSpec as P


def passed_along(value, axis, steps):
    count = lax.axis_size(axis)
    leading, last = (max(0, -steps), min(count, count - steps))
    return lax.ppermute(value, axis, [(source, source + steps) for source in range(leading, last)])


def swapped(value, axis):
    count = lax.axis_size(axis)
    return lax.ppermute(value, axis, [(source, count - 1 - source) for source in range(count)])


def convolve(source, kernel, flipped):
    if flipped:
        kernel = lax.rev(kernel, (0, 1, 2))
        layout = "DHWOI"
    else:
        layout = "DHWIO"
    return lax.conv_general_dilated(
        source,
        kernel,
        (1, 1, 1),
        [(0, 0), (1, 1), (1, 1)],
        dimension_numbers=("NDHWC", layout, "NDHWC"),
        preferred_element_type=jnp.float32,
    )


def kernel_terms(extended, cotangent):
    terms = lax.conv_general_dilated(
        extended,
        cotangent,
        (1, 1, 1),
        [(0, 0), (1, 1), (1, 1)],
        dimension_numbers=("CDHWN", "IDHWO", "NDHWC"),
        preferred_element_type=jnp.float32,
    )
    return jnp.transpose(terms, (1, 2, 3, 0, 4))


def channel_half(value, half, owners, pair):
    shape = value.shape
    split = value.reshape(shape[:-1] + (owners, pair, shape[-1] // (owners * pair)))
    taken = lax.dynamic_index_in_dim(split, half, axis=len(shape), keepdims=False)
    return taken.reshape(shape[:-1] + (owners * shape[-1] // (owners * pair),))


def shards(clips, kernel, cotangent):
    owners = lax.axis_size("tm")
    pair = lax.axis_size("dp")
    chans = clips.shape[-1]
    me = lax.axis_index("dp")
    wide = clips.astype(jnp.float32)
    act = jax.nn.silu(wide).astype(jnp.bfloat16)
    earlier = passed_along(act, "tm", 1)
    extended = jnp.concatenate([earlier, act], axis=1)
    following = passed_along(cotangent, "tm", -1)

    mine = channel_half(extended, me, owners, pair)
    theirs_for_me = swapped(channel_half(extended, pair - 1 - me, owners, pair), "dp")
    partner_cot = swapped(cotangent, "dp")
    both_ext = jnp.concatenate([mine, theirs_for_me], axis=0)
    both_cot = jnp.concatenate([cotangent, partner_cot], axis=0)
    terms = kernel_terms(both_ext, both_cot)
    terms = terms.reshape(terms.shape[:3] + (owners, chans // (owners * pair), chans))
    grad_kernel = lax.psum_scatter(terms, "tm", scatter_dimension=3, tiled=True)
    grad_kernel = grad_kernel.reshape(grad_kernel.shape[:3] + (chans // (owners * pair), chans))

    conv = convolve(extended, kernel, False)
    output = (wide + conv).astype(jnp.bfloat16)
    cot_ext = jnp.concatenate([cotangent, following], axis=1)
    grad_act = convolve(cot_ext, kernel, True)
    sig = jax.nn.sigmoid(wide)
    grad_input = (
        cotangent.astype(jnp.float32) + grad_act * sig * (1.0 + wide * (1.0 - sig))
    ).astype(jnp.bfloat16)
    return (output, grad_input, grad_kernel)


def solution(mesh):
    in_specs = (
        P(("groups", "dp"), "tm", None, None, None),
        P(),
        P(("groups", "dp"), "tm", None, None, None),
    )
    out_specs = (
        P(("groups", "dp"), "tm", None, None, None),
        P(("groups", "dp"), "tm", None, None, None),
        P("groups", None, None, ("tm", "dp"), None),
    )
    return jax.shard_map(shards, mesh=mesh, in_specs=in_specs, out_specs=out_specs, check_vma=False)
```

```python
import functools

import numpy as np

import jax
import jax.numpy as jnp
from jax import lax
from jax.sharding import PartitionSpec as P


def passed_along(value, axis, steps):
    count = lax.axis_size(axis)
    leading, last = (max(0, -steps), min(count, count - steps))
    return lax.ppermute(value, axis, [(source, source + steps) for source in range(leading, last)])


def swapped(value, axis):
    count = lax.axis_size(axis)
    return lax.ppermute(value, axis, [(source, count - 1 - source) for source in range(count)])


def ring_order(mesh, axis):
    devices = np.asarray(mesh.devices)
    at = mesh.axis_names.index(axis)
    count = devices.shape[at]
    line = [devices[tuple(i if d == at else 0 for d in range(devices.ndim))] for i in range(count)]
    try:
        coords = [tuple(d.coords) for d in line]
    except AttributeError:
        return list(range(count))

    def near(a, b):
        return sum(abs(x - y) for x, y in zip(coords[a], coords[b])) == 1

    best = [None]
    budget = [20000]

    def walk(path, seen):
        budget[0] -= 1
        if budget[0] < 0:
            return True
        if len(path) == count:
            if near(path[-1], path[0]):
                best[0] = list(path)
                return True
            if best[0] is None:
                best[0] = list(path)
            return False
        for nxt in range(count):
            if nxt not in seen and near(path[-1], nxt):
                path.append(nxt)
                seen.add(nxt)
                if walk(path, seen):
                    return True
                path.pop()
                seen.discard(nxt)
        return False

    walk([0], {0})
    return best[0] if best[0] is not None else list(range(count))


def ring_reduce_scatter(terms, axis, order, direction):
    count = len(order)
    place = [0] * count
    for position, owner in enumerate(order):
        place[owner] = position
    me = jnp.asarray(place, jnp.int32)[lax.axis_index(axis)]
    owners = jnp.asarray(order, jnp.int32)
    pairs = [(order[q], order[(q + direction) % count]) for q in range(count)]

    def own(step):
        chunk = (me - direction * (step + 1) + 2 * count) % count
        return lax.dynamic_index_in_dim(terms, owners[chunk], axis=0, keepdims=False)

    total = own(0)
    for step in range(count - 1):
        total = lax.ppermute(total, axis, pairs) + own(step + 1)
    return total


def convolve(source, kernel, flipped):
    if flipped:
        kernel = lax.rev(kernel, (0, 1, 2))
        layout = "DHWOI"
    else:
        layout = "DHWIO"
    return lax.conv_general_dilated(
        source,
        kernel,
        (1, 1, 1),
        [(0, 0), (1, 1), (1, 1)],
        dimension_numbers=("NDHWC", layout, "NDHWC"),
        preferred_element_type=jnp.float32,
    )


def kernel_terms(extended, cotangent):
    return lax.conv_general_dilated(
        extended,
        cotangent,
        (1, 1, 1),
        [(0, 0), (1, 1), (1, 1)],
        dimension_numbers=("CDHWN", "IDHWO", "NDHWC"),
        preferred_element_type=jnp.float32,
    )


def channel_half(value, half, owners, pair):
    shape = value.shape
    split = value.reshape(shape[:-1] + (owners, pair, shape[-1] // (owners * pair)))
    taken = lax.dynamic_index_in_dim(split, half, axis=len(shape), keepdims=False)
    return taken.reshape(shape[:-1] + (owners * shape[-1] // (owners * pair),))


def shards(order, clips, kernel, cotangent):
    owners = lax.axis_size("tm")
    pair = lax.axis_size("dp")
    chans = clips.shape[-1]
    me = lax.axis_index("dp")
    wide = clips.astype(jnp.float32)
    act = jax.nn.silu(wide).astype(jnp.bfloat16)
    earlier = passed_along(act, "tm", 1)
    extended = jnp.concatenate([earlier, act], axis=1)
    following = passed_along(cotangent, "tm", -1)

    mine = channel_half(extended, me, owners, pair)
    theirs_for_me = swapped(channel_half(extended, pair - 1 - me, owners, pair), "dp")
    partner_cot = swapped(cotangent, "dp")
    both_ext = jnp.concatenate([mine, theirs_for_me], axis=0)
    both_cot = jnp.concatenate([cotangent, partner_cot], axis=0)
    terms = kernel_terms(both_ext, both_cot)
    terms = terms.reshape((owners, chans // (owners * pair)) + terms.shape[1:])
    split = chans // 2
    forward = ring_reduce_scatter(terms[..., :split], "tm", order, 1)
    backward = ring_reduce_scatter(terms[..., split:], "tm", order, -1)
    grad_kernel = jnp.transpose(jnp.concatenate([forward, backward], axis=-1), (1, 2, 3, 0, 4))

    conv = convolve(extended, kernel, False)
    output = (wide + conv).astype(jnp.bfloat16)
    cot_ext = jnp.concatenate([cotangent, following], axis=1)
    grad_act = convolve(cot_ext, kernel, True)
    sig = jax.nn.sigmoid(wide)
    grad_input = (
        cotangent.astype(jnp.float32) + grad_act * sig * (1.0 + wide * (1.0 - sig))
    ).astype(jnp.bfloat16)
    return (output, grad_input, grad_kernel)


def solution(mesh):
    in_specs = (
        P(("groups", "dp"), "tm", None, None, None),
        P(),
        P(("groups", "dp"), "tm", None, None, None),
    )
    out_specs = (
        P(("groups", "dp"), "tm", None, None, None),
        P(("groups", "dp"), "tm", None, None, None),
        P("groups", None, None, ("tm", "dp"), None),
    )
    order = ring_order(mesh, "tm")
    return jax.shard_map(functools.partial(shards, order), mesh=mesh, in_specs=in_specs, out_specs=out_specs, check_vma=False)
```

```python
import functools

import numpy as np

import jax
import jax.numpy as jnp
from jax import lax
from jax.sharding import PartitionSpec as P


def passed_along(value, axis, steps):
    count = lax.axis_size(axis)
    leading, last = (max(0, -steps), min(count, count - steps))
    return lax.ppermute(value, axis, [(source, source + steps) for source in range(leading, last)])


def swapped(value, axis):
    count = lax.axis_size(axis)
    return lax.ppermute(value, axis, [(source, count - 1 - source) for source in range(count)])


def ring_order(mesh, axis):
    devices = np.asarray(mesh.devices)
    at = mesh.axis_names.index(axis)
    count = devices.shape[at]
    line = [devices[tuple(i if d == at else 0 for d in range(devices.ndim))] for i in range(count)]
    try:
        coords = [tuple(d.coords) for d in line]
    except AttributeError:
        return list(range(count))

    def near(a, b):
        return sum(abs(x - y) for x, y in zip(coords[a], coords[b])) == 1

    best = [None]
    budget = [20000]

    def walk(path, seen):
        budget[0] -= 1
        if budget[0] < 0:
            return True
        if len(path) == count:
            if near(path[-1], path[0]):
                best[0] = list(path)
                return True
            if best[0] is None:
                best[0] = list(path)
            return False
        for nxt in range(count):
            if nxt not in seen and near(path[-1], nxt):
                path.append(nxt)
                seen.add(nxt)
                if walk(path, seen):
                    return True
                path.pop()
                seen.discard(nxt)
        return False

    walk([0], {0})
    return best[0] if best[0] is not None else list(range(count))


def ring_reduce_scatter(terms, axis, order, direction):
    count = len(order)
    place = [0] * count
    for position, owner in enumerate(order):
        place[owner] = position
    me = jnp.asarray(place, jnp.int32)[lax.axis_index(axis)]
    owners = jnp.asarray(order, jnp.int32)
    pairs = [(order[q], order[(q + direction) % count]) for q in range(count)]

    def own(step):
        chunk = (me - direction * (step + 1) + 2 * count) % count
        return lax.dynamic_index_in_dim(terms, owners[chunk], axis=0, keepdims=False)

    total = own(0)
    for step in range(count - 1):
        total = lax.ppermute(total, axis, pairs) + own(step + 1)
    return total


def convolve(source, kernel, flipped):
    if flipped:
        kernel = lax.rev(kernel, (0, 1, 2))
        layout = "DHWOI"
    else:
        layout = "DHWIO"
    return lax.conv_general_dilated(
        source,
        kernel,
        (1, 1, 1),
        [(0, 0), (1, 1), (1, 1)],
        dimension_numbers=("NDHWC", layout, "NDHWC"),
        preferred_element_type=jnp.float32,
    )


def kernel_terms(extended, cotangent):
    return lax.conv_general_dilated(
        extended,
        cotangent,
        (1, 1, 1),
        [(0, 0), (1, 1), (1, 1)],
        dimension_numbers=("CDHWN", "IDHWO", "NDHWC"),
        preferred_element_type=jnp.float32,
    )


def shards(order, clips, kernel, cotangent):
    owners = lax.axis_size("tm")
    pair = lax.axis_size("dp")
    chans = clips.shape[-1]
    me = lax.axis_index("dp")
    wide = clips.astype(jnp.float32)
    act = jax.nn.silu(wide).astype(jnp.bfloat16)
    earlier = passed_along(act, "tm", 1)
    extended = jnp.concatenate([earlier, act], axis=1)
    following = passed_along(cotangent, "tm", -1)

    terms = kernel_terms(extended, cotangent)
    terms = terms.reshape((owners, pair, chans // (owners * pair)) + terms.shape[1:])
    mine = lax.dynamic_index_in_dim(terms, me, axis=1, keepdims=False)
    theirs = lax.dynamic_index_in_dim(terms, pair - 1 - me, axis=1, keepdims=False)
    terms = mine + swapped(theirs, "dp")
    split = chans // 2
    forward = ring_reduce_scatter(terms[..., :split], "tm", order, 1)
    backward = ring_reduce_scatter(terms[..., split:], "tm", order, -1)
    grad_kernel = jnp.transpose(jnp.concatenate([forward, backward], axis=-1), (1, 2, 3, 0, 4))

    conv = convolve(extended, kernel, False)
    output = (wide + conv).astype(jnp.bfloat16)
    cot_ext = jnp.concatenate([cotangent, following], axis=1)
    grad_act = convolve(cot_ext, kernel, True)
    sig = jax.nn.sigmoid(wide)
    grad_input = (
        cotangent.astype(jnp.float32) + grad_act * sig * (1.0 + wide * (1.0 - sig))
    ).astype(jnp.bfloat16)
    return (output, grad_input, grad_kernel)


def solution(mesh):
    in_specs = (
        P(("groups", "dp"), "tm", None, None, None),
        P(),
        P(("groups", "dp"), "tm", None, None, None),
    )
    out_specs = (
        P(("groups", "dp"), "tm", None, None, None),
        P(("groups", "dp"), "tm", None, None, None),
        P("groups", None, None, ("tm", "dp"), None),
    )
    order = ring_order(mesh, "tm")
    return jax.shard_map(functools.partial(shards, order), mesh=mesh, in_specs=in_specs, out_specs=out_specs, check_vma=False)
```

```python
import functools

import numpy as np

import jax
import jax.numpy as jnp
from jax import lax
from jax.sharding import PartitionSpec as P


def passed_along(value, axis, steps):
    count = lax.axis_size(axis)
    leading, last = (max(0, -steps), min(count, count - steps))
    return lax.ppermute(value, axis, [(source, source + steps) for source in range(leading, last)])


def swapped(value, axis):
    count = lax.axis_size(axis)
    return lax.ppermute(value, axis, [(source, count - 1 - source) for source in range(count)])


def ring_order(mesh, axis):
    devices = np.asarray(mesh.devices)
    at = mesh.axis_names.index(axis)
    count = devices.shape[at]
    line = [devices[tuple(i if d == at else 0 for d in range(devices.ndim))] for i in range(count)]
    try:
        coords = [tuple(d.coords) for d in line]
    except AttributeError:
        return list(range(count))

    def near(a, b):
        return sum(abs(x - y) for x, y in zip(coords[a], coords[b])) == 1

    best = [None]
    budget = [20000]

    def walk(path, seen):
        budget[0] -= 1
        if budget[0] < 0:
            return True
        if len(path) == count:
            if near(path[-1], path[0]):
                best[0] = list(path)
                return True
            if best[0] is None:
                best[0] = list(path)
            return False
        for nxt in range(count):
            if nxt not in seen and near(path[-1], nxt):
                path.append(nxt)
                seen.add(nxt)
                if walk(path, seen):
                    return True
                path.pop()
                seen.discard(nxt)
        return False

    walk([0], {0})
    return best[0] if best[0] is not None else list(range(count))


def ring_reduce_scatter(terms, axis, order, fillers):
    count = len(order)
    place = [0] * count
    for position, owner in enumerate(order):
        place[owner] = position
    me = jnp.asarray(place, jnp.int32)[lax.axis_index(axis)]
    owners = jnp.asarray(order, jnp.int32)
    split = terms.shape[-1] // 2
    halves = (terms[..., :split], terms[..., split:])
    directions = (1, -1)
    pairs = [[(order[q], order[(q + d) % count]) for q in range(count)] for d in directions]

    def own(k, step):
        chunk = (me - directions[k] * (step + 1) + 2 * count) % count
        return lax.dynamic_index_in_dim(halves[k], owners[chunk], axis=1, keepdims=False)

    totals = [own(0, 0), own(1, 0)]
    done = {}
    for step in range(count - 1):
        filler = fillers.get(step)
        if filler is not None:
            work, operands = filler
            *totals, operands = lax.optimization_barrier((*totals, operands))
        arrived = [lax.ppermute(totals[k], axis, pairs[k]) for k in range(2)]
        if filler is not None:
            *arrived, done[step] = lax.optimization_barrier((*arrived, work(*operands)))
        totals = [arrived[k] + own(k, step + 1) for k in range(2)]
    return jnp.concatenate(totals, axis=-1), done


def convolve(source, kernel, flipped):
    if flipped:
        kernel = lax.rev(kernel, (0, 1, 2))
        layout = "DHWOI"
    else:
        layout = "DHWIO"
    return lax.conv_general_dilated(
        source,
        kernel,
        (1, 1, 1),
        [(0, 0), (1, 1), (1, 1)],
        dimension_numbers=("NDHWC", layout, "NDHWC"),
        preferred_element_type=jnp.float32,
    )


def kernel_terms(extended, cotangent):
    frames, height, width, chans = cotangent.shape[1:]
    spaced = jnp.pad(extended, ((0, 0), (0, 0), (1, 1), (1, 1), (0, 0)))
    columns = jnp.concatenate(
        [spaced[:, :, kh : kh + height, kw : kw + width, :] for kh in range(3) for kw in range(3)], axis=-1
    )
    columns = columns.reshape(columns.shape[:2] + (height * width, 9 * chans))
    flat_grad = cotangent.reshape(-1, chans)
    pieces = [
        lax.dot_general(
            columns[:, kt : kt + frames].reshape(-1, 9 * chans),
            flat_grad,
            (((0,), (0,)), ((), ())),
            preferred_element_type=jnp.float32,
        )
        for kt in range(3)
    ]
    return jnp.stack(pieces).reshape(27, chans, chans)


def shards(order, clips, kernel, cotangent):
    owners = lax.axis_size("tm")
    pair = lax.axis_size("dp")
    chans = clips.shape[-1]
    me = lax.axis_index("dp")
    wide = clips.astype(jnp.float32)
    act = jax.nn.silu(wide).astype(jnp.bfloat16)
    earlier = passed_along(act, "tm", 1)
    earlier, sent_cot = lax.optimization_barrier((earlier, cotangent))
    following = passed_along(sent_cot, "tm", -1)
    extended = jnp.concatenate([earlier, act], axis=1)

    terms = kernel_terms(extended, cotangent)
    terms = terms.reshape((27, owners, pair, chans // (owners * pair), chans))
    mine = lax.dynamic_index_in_dim(terms, me, axis=2, keepdims=False)
    theirs = lax.dynamic_index_in_dim(terms, pair - 1 - me, axis=2, keepdims=False)
    terms = mine + swapped(theirs, "dp")

    def forward_pass(extended, wide):
        conv = convolve(extended, kernel, False)
        return (wide + conv).astype(jnp.bfloat16)

    def backward_pass(cotangent, following, wide):
        cot_ext = jnp.concatenate([cotangent, following], axis=1)
        grad_act = convolve(cot_ext, kernel, True)
        sig = jax.nn.sigmoid(wide)
        return (
            cotangent.astype(jnp.float32) + grad_act * sig * (1.0 + wide * (1.0 - sig))
        ).astype(jnp.bfloat16)

    fillers = {1: (forward_pass, (extended, wide)), 3: (backward_pass, (cotangent, following, wide))}
    grad_kernel, done = ring_reduce_scatter(terms, "tm", order, fillers)
    grad_kernel = grad_kernel.reshape((3, 3, 3) + grad_kernel.shape[1:])
    return (done[1], done[3], grad_kernel)


def solution(mesh):
    in_specs = (
        P(("groups", "dp"), "tm", None, None, None),
        P(),
        P(("groups", "dp"), "tm", None, None, None),
    )
    out_specs = (
        P(("groups", "dp"), "tm", None, None, None),
        P(("groups", "dp"), "tm", None, None, None),
        P("groups", None, None, ("tm", "dp"), None),
    )
    order = ring_order(mesh, "tm")
    return jax.shard_map(functools.partial(shards, order), mesh=mesh, in_specs=in_specs, out_specs=out_specs, check_vma=False)
```

```python
import jax
import jax.numpy as jnp
from jax import lax
from jax.sharding import PartitionSpec as P


def passed_along(value, axis, steps):
    count = lax.axis_size(axis)
    leading, last = (max(0, -steps), min(count, count - steps))
    return lax.ppermute(value, axis, [(source, source + steps) for source in range(leading, last)])


def convolve(source, kernel, flipped):
    if flipped:
        kernel = lax.rev(kernel, (0, 1, 2))
        layout = "DHWOI"
    else:
        layout = "DHWIO"
    return lax.conv_general_dilated(
        source,
        kernel,
        (1, 1, 1),
        [(0, 0), (1, 1), (1, 1)],
        dimension_numbers=("NDHWC", layout, "NDHWC"),
        preferred_element_type=jnp.float32,
    )


def kernel_terms(extended, cotangent):
    frames, height, width, chans = cotangent.shape[1:]
    spaced = jnp.pad(extended, ((0, 0), (0, 0), (1, 1), (1, 1), (0, 0)))
    columns = jnp.concatenate(
        [spaced[:, :, kh : kh + height, kw : kw + width, :] for kh in range(3) for kw in range(3)], axis=-1
    )
    columns = columns.reshape(columns.shape[:2] + (height * width, 9 * chans))
    flat_grad = cotangent.reshape(-1, chans)
    pieces = [
        lax.dot_general(
            columns[:, kt : kt + frames].reshape(-1, 9 * chans),
            flat_grad,
            (((0,), (0,)), ((), ())),
            preferred_element_type=jnp.float32,
        )
        for kt in range(3)
    ]
    return jnp.stack(pieces).reshape(27, chans, chans)


def shards(clips, kernel, cotangent):
    wide = clips.astype(jnp.float32)
    act = jax.nn.silu(wide).astype(jnp.bfloat16)
    earlier = passed_along(act, "tm", 1)
    earlier, sent_cot = lax.optimization_barrier((earlier, cotangent))
    following = passed_along(sent_cot, "tm", -1)
    extended = jnp.concatenate([earlier, act], axis=1)

    terms = kernel_terms(extended, cotangent)
    terms = terms.reshape((3, 3, 3) + terms.shape[1:])
    grad_kernel = lax.psum_scatter(terms, ("tm", "dp"), scatter_dimension=3, tiled=True)

    conv = convolve(extended, kernel, False)
    output = (wide + conv).astype(jnp.bfloat16)
    cot_ext = jnp.concatenate([cotangent, following], axis=1)
    grad_act = convolve(cot_ext, kernel, True)
    sig = jax.nn.sigmoid(wide)
    grad_input = (
        cotangent.astype(jnp.float32) + grad_act * sig * (1.0 + wide * (1.0 - sig))
    ).astype(jnp.bfloat16)
    return (output, grad_input, grad_kernel)


def solution(mesh):
    in_specs = (
        P(("groups", "dp"), "tm", None, None, None),
        P(),
        P(("groups", "dp"), "tm", None, None, None),
    )
    out_specs = (
        P(("groups", "dp"), "tm", None, None, None),
        P(("groups", "dp"), "tm", None, None, None),
        P("groups", None, None, ("tm", "dp"), None),
    )
    return jax.shard_map(shards, mesh=mesh, in_specs=in_specs, out_specs=out_specs, check_vma=False)
```

```python
import jax
import jax.numpy as jnp
from jax import lax
from jax.sharding import PartitionSpec as P


def passed_along(value, axis, steps):
    count = lax.axis_size(axis)
    leading, last = (max(0, -steps), min(count, count - steps))
    return lax.ppermute(value, axis, [(source, source + steps) for source in range(leading, last)])


def convolve(source, kernel, time_pad, flipped):
    if flipped:
        kernel = lax.rev(kernel, (0, 1, 2))
        layout = "DHWOI"
    else:
        layout = "DHWIO"
    return lax.conv_general_dilated(
        source,
        kernel,
        (1, 1, 1),
        [time_pad, (1, 1), (1, 1)],
        dimension_numbers=("NDHWC", layout, "NDHWC"),
        preferred_element_type=jnp.float32,
    )


def kernel_terms(extended, cotangent):
    frames, height, width, chans = cotangent.shape[1:]
    spaced = jnp.pad(extended, ((0, 0), (0, 0), (1, 1), (1, 1), (0, 0)))
    columns = jnp.concatenate(
        [spaced[:, :, kh : kh + height, kw : kw + width, :] for kh in range(3) for kw in range(3)], axis=-1
    )
    columns = columns.reshape(columns.shape[:2] + (height * width, 9 * chans))
    flat_grad = cotangent.reshape(-1, chans)
    pieces = [
        lax.dot_general(
            flat_grad,
            columns[:, kt : kt + frames].reshape(-1, 9 * chans),
            (((0,), (0,)), ((), ())),
            preferred_element_type=jnp.float32,
        )
        for kt in range(3)
    ]
    return jnp.transpose(jnp.stack(pieces).reshape(3, chans, 9, chans), (0, 2, 3, 1)).reshape(27, chans, chans)


def shards(clips, kernel, cotangent):
    frames = clips.shape[1]
    wide = clips.astype(jnp.float32)
    act = jax.nn.silu(wide).astype(jnp.bfloat16)
    earlier = passed_along(act, "tm", 1)
    extended = jnp.concatenate([earlier, act], axis=1)
    conv = convolve(extended, kernel, (0, 0), False)
    output = (wide + conv).astype(jnp.bfloat16)
    padded_grad = jnp.pad(cotangent, ((0, 0), (2, 2), (0, 0), (0, 0), (0, 0)))
    partial_grad = convolve(padded_grad, kernel, (0, 0), True)
    returned = passed_along(partial_grad[:, :2].astype(jnp.bfloat16), "tm", -1).astype(jnp.float32)
    returned = jnp.pad(returned, ((0, 0), (0, frames - 2), (0, 0), (0, 0), (0, 0)))
    grad_act = partial_grad[:, 2:] + returned
    sig = jax.nn.sigmoid(wide)
    grad_input = (
        cotangent.astype(jnp.float32) + grad_act * sig * (1.0 + wide * (1.0 - sig))
    ).astype(jnp.bfloat16)
    terms = kernel_terms(extended, cotangent).reshape((3, 3, 3) + (cotangent.shape[-1],) * 2)
    grad_kernel = lax.psum_scatter(terms, ("tm", "dp"), scatter_dimension=3, tiled=True)
    return (output, grad_input, grad_kernel)


def solution(mesh):
    in_specs = (
        P(("groups", "dp"), "tm", None, None, None),
        P(),
        P(("groups", "dp"), "tm", None, None, None),
    )
    out_specs = (
        P(("groups", "dp"), "tm", None, None, None),
        P(("groups", "dp"), "tm", None, None, None),
        P("groups", None, None, ("tm", "dp"), None),
    )
    return jax.shard_map(shards, mesh=mesh, in_specs=in_specs, out_specs=out_specs, check_vma=False)
```

```python
import functools

import numpy as np

import jax
import jax.numpy as jnp
from jax import lax
from jax.sharding import PartitionSpec as P


def passed_along(value, axis, steps):
    count = lax.axis_size(axis)
    leading, last = (max(0, -steps), min(count, count - steps))
    return lax.ppermute(value, axis, [(source, source + steps) for source in range(leading, last)])


def swapped(value, axis):
    count = lax.axis_size(axis)
    return lax.ppermute(value, axis, [(source, count - 1 - source) for source in range(count)])


def ring_order(mesh, axis):
    devices = np.asarray(mesh.devices)
    at = mesh.axis_names.index(axis)
    count = devices.shape[at]
    line = [devices[tuple(i if d == at else 0 for d in range(devices.ndim))] for i in range(count)]
    try:
        coords = [tuple(d.coords) for d in line]
    except AttributeError:
        return list(range(count))

    def near(a, b):
        return sum(abs(x - y) for x, y in zip(coords[a], coords[b])) == 1

    best = [None]
    budget = [20000]

    def walk(path, seen):
        budget[0] -= 1
        if budget[0] < 0:
            return True
        if len(path) == count:
            if near(path[-1], path[0]):
                best[0] = list(path)
                return True
            if best[0] is None:
                best[0] = list(path)
            return False
        for nxt in range(count):
            if nxt not in seen and near(path[-1], nxt):
                path.append(nxt)
                seen.add(nxt)
                if walk(path, seen):
                    return True
                path.pop()
                seen.discard(nxt)
        return False

    walk([0], {0})
    return best[0] if best[0] is not None else list(range(count))


def ring_reduce_scatter(terms, axis, order, direction):
    count = len(order)
    place = [0] * count
    for position, owner in enumerate(order):
        place[owner] = position
    me = jnp.asarray(place, jnp.int32)[lax.axis_index(axis)]
    owners = jnp.asarray(order, jnp.int32)
    pairs = [(order[q], order[(q + direction) % count]) for q in range(count)]

    def own(step):
        chunk = (me - direction * (step + 1) + 2 * count) % count
        return lax.dynamic_index_in_dim(terms, owners[chunk], axis=1, keepdims=False)

    total = own(0)
    for step in range(count - 1):
        total = lax.ppermute(total, axis, pairs) + own(step + 1)
    return total


def convolve(source, kernel, flipped):
    if flipped:
        kernel = lax.rev(kernel, (0, 1, 2))
        layout = "DHWOI"
    else:
        layout = "DHWIO"
    return lax.conv_general_dilated(
        source,
        kernel,
        (1, 1, 1),
        [(0, 0), (1, 1), (1, 1)],
        dimension_numbers=("NDHWC", layout, "NDHWC"),
        preferred_element_type=jnp.float32,
    )


def kernel_terms(extended, cotangent):
    frames, height, width, chans = cotangent.shape[1:]
    spaced = jnp.pad(extended, ((0, 0), (0, 0), (1, 1), (1, 1), (0, 0)))
    columns = jnp.concatenate(
        [spaced[:, :, kh : kh + height, kw : kw + width, :] for kh in range(3) for kw in range(3)], axis=-1
    )
    columns = columns.reshape(columns.shape[:2] + (height * width, 9 * chans))
    flat_grad = cotangent.reshape(-1, chans)
    pieces = [
        lax.dot_general(
            flat_grad,
            columns[:, kt : kt + frames].reshape(-1, 9 * chans),
            (((0,), (0,)), ((), ())),
            preferred_element_type=jnp.float32,
        )
        for kt in range(3)
    ]
    return jnp.transpose(jnp.stack(pieces).reshape(3, chans, 9, chans), (0, 2, 3, 1)).reshape(27, chans, chans)


def shards(order, clips, kernel, cotangent):
    owners = lax.axis_size("tm")
    pair = lax.axis_size("dp")
    chans = clips.shape[-1]
    me = lax.axis_index("dp")
    wide = clips.astype(jnp.float32)
    act = jax.nn.silu(wide).astype(jnp.bfloat16)
    earlier = passed_along(act, "tm", 1)
    extended = jnp.concatenate([earlier, act], axis=1)
    following = passed_along(cotangent, "tm", -1)

    terms = kernel_terms(extended, cotangent)
    terms = terms.reshape((27, owners, pair, chans // (owners * pair), chans))
    mine = lax.dynamic_index_in_dim(terms, me, axis=2, keepdims=False)
    theirs = lax.dynamic_index_in_dim(terms, pair - 1 - me, axis=2, keepdims=False)
    terms = mine + swapped(theirs, "dp")
    split = chans // 2
    forward = ring_reduce_scatter(terms[..., :split], "tm", order, 1)
    backward = ring_reduce_scatter(terms[..., split:], "tm", order, -1)
    grad_kernel = jnp.concatenate([forward, backward], axis=-1).reshape((3, 3, 3, chans // (owners * pair), chans))

    conv = convolve(extended, kernel, False)
    output = (wide + conv).astype(jnp.bfloat16)
    cot_ext = jnp.concatenate([cotangent, following], axis=1)
    grad_act = convolve(cot_ext, kernel, True)
    sig = jax.nn.sigmoid(wide)
    grad_input = (
        cotangent.astype(jnp.float32) + grad_act * sig * (1.0 + wide * (1.0 - sig))
    ).astype(jnp.bfloat16)
    return (output, grad_input, grad_kernel)


def solution(mesh):
    in_specs = (
        P(("groups", "dp"), "tm", None, None, None),
        P(),
        P(("groups", "dp"), "tm", None, None, None),
    )
    out_specs = (
        P(("groups", "dp"), "tm", None, None, None),
        P(("groups", "dp"), "tm", None, None, None),
        P("groups", None, None, ("tm", "dp"), None),
    )
    order = ring_order(mesh, "tm")
    return jax.shard_map(functools.partial(shards, order), mesh=mesh, in_specs=in_specs, out_specs=out_specs, check_vma=False)
```

```python
import jax
import jax.numpy as jnp
from jax import lax
from jax.sharding import PartitionSpec as P


def passed_along(value, axis, steps):
    count = lax.axis_size(axis)
    leading, last = (max(0, -steps), min(count, count - steps))
    return lax.ppermute(value, axis, [(source, source + steps) for source in range(leading, last)])


def convolve(source, kernel, time_pad, flipped):
    if flipped:
        kernel = lax.rev(kernel, (0, 1, 2))
        layout = "DHWOI"
    else:
        layout = "DHWIO"
    return lax.conv_general_dilated(
        source,
        kernel,
        (1, 1, 1),
        [time_pad, (1, 1), (1, 1)],
        dimension_numbers=("NDHWC", layout, "NDHWC"),
        preferred_element_type=jnp.float32,
    )


def kernel_terms(extended, own, cotangent):
    frames = cotangent.shape[1]
    height = cotangent.shape[2]
    width = cotangent.shape[3]
    chans = cotangent.shape[4]
    spaced = jnp.pad(extended, ((0, 0), (0, 0), (1, 1), (1, 1), (0, 0)))
    spaced_own = jnp.pad(own, ((0, 0), (0, 0), (1, 1), (1, 1), (0, 0)))
    flat_grad = cotangent.reshape(-1, chans)
    pieces = {}
    for kt in (2, 1, 0):
        for kh in range(3):
            for kw in range(3):
                if kt == 2:
                    window = spaced_own[:, :, kh : kh + height, kw : kw + width, :]
                else:
                    window = spaced[:, kt : kt + frames, kh : kh + height, kw : kw + width, :]
                window = window.reshape(-1, chans)
                pieces[kt, kh, kw] = lax.dot_general(
                    window,
                    flat_grad,
                    (((0,), (0,)), ((), ())),
                    preferred_element_type=jnp.float32,
                )
    pieces = [pieces[kt, kh, kw] for kt in (2, 1, 0) for kh in range(3) for kw in range(3)]
    return jnp.stack(pieces).reshape(3, 3, 3, chans, chans)


def shards(clips, kernel, cotangent):
    frames = clips.shape[1]
    wide = clips.astype(jnp.float32)
    act = jax.nn.silu(wide).astype(jnp.bfloat16)
    earlier = passed_along(act, "tm", 1)
    extended = jnp.concatenate([earlier, act], axis=1)
    conv = convolve(extended, kernel, (0, 0), False)
    output = (wide + conv).astype(jnp.bfloat16)
    padded_grad = jnp.pad(cotangent, ((0, 0), (2, 2), (0, 0), (0, 0), (0, 0)))
    partial_grad = convolve(padded_grad, kernel, (0, 0), True)
    returned = passed_along(partial_grad[:, :2].astype(jnp.bfloat16), "tm", -1).astype(jnp.float32)
    returned = jnp.pad(returned, ((0, 0), (0, frames - 2), (0, 0), (0, 0), (0, 0)))
    grad_act = partial_grad[:, 2:] + returned
    sig = jax.nn.sigmoid(wide)
    grad_input = (
        cotangent.astype(jnp.float32) + grad_act * sig * (1.0 + wide * (1.0 - sig))
    ).astype(jnp.bfloat16)
    terms = kernel_terms(extended, act, cotangent)
    grad_kernel = lax.rev(lax.psum_scatter(terms, ("tm", "dp"), scatter_dimension=3, tiled=True), (0,))
    return (output, grad_input, grad_kernel)


def solution(mesh):
    in_specs = (
        P(("groups", "dp"), "tm", None, None, None),
        P(),
        P(("groups", "dp"), "tm", None, None, None),
    )
    out_specs = (
        P(("groups", "dp"), "tm", None, None, None),
        P(("groups", "dp"), "tm", None, None, None),
        P("groups", None, None, ("tm", "dp"), None),
    )
    return jax.shard_map(shards, mesh=mesh, in_specs=in_specs, out_specs=out_specs, check_vma=False)
```

```python
import functools

import numpy as np

import jax
import jax.numpy as jnp
from jax import lax
from jax.sharding import PartitionSpec as P


def passed_along(value, axis, steps):
    count = lax.axis_size(axis)
    leading, last = (max(0, -steps), min(count, count - steps))
    return lax.ppermute(value, axis, [(source, source + steps) for source in range(leading, last)])


def swapped(value, axis):
    count = lax.axis_size(axis)
    return lax.ppermute(value, axis, [(source, count - 1 - source) for source in range(count)])


def ring_order(mesh, axis):
    devices = np.asarray(mesh.devices)
    at = mesh.axis_names.index(axis)
    count = devices.shape[at]
    line = [devices[tuple(i if d == at else 0 for d in range(devices.ndim))] for i in range(count)]
    try:
        coords = [tuple(d.coords) for d in line]
    except AttributeError:
        return list(range(count))

    def near(a, b):
        return sum(abs(x - y) for x, y in zip(coords[a], coords[b])) == 1

    best = [None]
    budget = [20000]

    def walk(path, seen):
        budget[0] -= 1
        if budget[0] < 0:
            return True
        if len(path) == count:
            if near(path[-1], path[0]):
                best[0] = list(path)
                return True
            if best[0] is None:
                best[0] = list(path)
            return False
        for nxt in range(count):
            if nxt not in seen and near(path[-1], nxt):
                path.append(nxt)
                seen.add(nxt)
                if walk(path, seen):
                    return True
                path.pop()
                seen.discard(nxt)
        return False

    walk([0], {0})
    return best[0] if best[0] is not None else list(range(count))


def ring_reduce_scatter(terms, axis, order, direction):
    count = len(order)
    place = [0] * count
    for position, owner in enumerate(order):
        place[owner] = position
    me = jnp.asarray(place, jnp.int32)[lax.axis_index(axis)]
    owners = jnp.asarray(order, jnp.int32)
    pairs = [(order[q], order[(q + direction) % count]) for q in range(count)]

    def own(step):
        chunk = (me - direction * (step + 1) + 2 * count) % count
        return lax.dynamic_index_in_dim(terms, owners[chunk], axis=1, keepdims=False)

    total = own(0)
    for step in range(count - 1):
        total = lax.ppermute(total, axis, pairs) + own(step + 1)
    return total


def convolve(source, kernel, time_pad, flipped):
    if flipped:
        kernel = lax.rev(kernel, (0, 1, 2))
        layout = "DHWOI"
    else:
        layout = "DHWIO"
    return lax.conv_general_dilated(
        source,
        kernel,
        (1, 1, 1),
        [time_pad, (1, 1), (1, 1)],
        dimension_numbers=("NDHWC", layout, "NDHWC"),
        preferred_element_type=jnp.float32,
    )


def kernel_terms(extended, own, cotangent):
    frames = cotangent.shape[1]
    height = cotangent.shape[2]
    width = cotangent.shape[3]
    chans = cotangent.shape[4]
    spaced = jnp.pad(extended, ((0, 0), (0, 0), (1, 1), (1, 1), (0, 0)))
    spaced_own = jnp.pad(own, ((0, 0), (0, 0), (1, 1), (1, 1), (0, 0)))
    flat_grad = cotangent.reshape(-1, chans)
    pieces = {}
    for kt in (2, 1, 0):
        for kh in range(3):
            for kw in range(3):
                if kt == 2:
                    window = spaced_own[:, :, kh : kh + height, kw : kw + width, :]
                else:
                    window = spaced[:, kt : kt + frames, kh : kh + height, kw : kw + width, :]
                window = window.reshape(-1, chans)
                pieces[kt, kh, kw] = lax.dot_general(
                    window,
                    flat_grad,
                    (((0,), (0,)), ((), ())),
                    preferred_element_type=jnp.float32,
                )
    pieces = [pieces[kt, kh, kw] for kt in (2, 1, 0) for kh in range(3) for kw in range(3)]
    return jnp.stack(pieces).reshape(3, 3, 3, chans, chans)


def shards(order, clips, kernel, cotangent):
    frames = clips.shape[1]
    wide = clips.astype(jnp.float32)
    act = jax.nn.silu(wide).astype(jnp.bfloat16)
    earlier = passed_along(act, "tm", 1)
    extended = jnp.concatenate([earlier, act], axis=1)
    conv = convolve(extended, kernel, (0, 0), False)
    output = (wide + conv).astype(jnp.bfloat16)
    padded_grad = jnp.pad(cotangent, ((0, 0), (2, 2), (0, 0), (0, 0), (0, 0)))
    partial_grad = convolve(padded_grad, kernel, (0, 0), True)
    returned = passed_along(partial_grad[:, :2].astype(jnp.bfloat16), "tm", -1).astype(jnp.float32)
    returned = jnp.pad(returned, ((0, 0), (0, frames - 2), (0, 0), (0, 0), (0, 0)))
    grad_act = partial_grad[:, 2:] + returned
    sig = jax.nn.sigmoid(wide)
    grad_input = (
        cotangent.astype(jnp.float32) + grad_act * sig * (1.0 + wide * (1.0 - sig))
    ).astype(jnp.bfloat16)
    terms = kernel_terms(extended, act, cotangent)
    owners = lax.axis_size("tm")
    pair = lax.axis_size("dp")
    chans = terms.shape[-1]
    me = lax.axis_index("dp")
    terms = lax.optimization_barrier(terms)
    terms = terms.reshape((27, owners, pair, chans // (owners * pair), chans))
    mine = lax.dynamic_index_in_dim(terms, me, axis=2, keepdims=False)
    theirs = lax.dynamic_index_in_dim(terms, pair - 1 - me, axis=2, keepdims=False)
    terms = mine + swapped(theirs, "dp")
    split = chans // 2
    forward = ring_reduce_scatter(terms[..., :split], "tm", order, 1)
    backward = ring_reduce_scatter(terms[..., split:], "tm", order, -1)
    grad_kernel = jnp.concatenate([forward, backward], axis=-1)
    grad_kernel = lax.rev(grad_kernel.reshape((3, 3, 3) + grad_kernel.shape[1:]), (0,))
    return (output, grad_input, grad_kernel)


def solution(mesh):
    in_specs = (
        P(("groups", "dp"), "tm", None, None, None),
        P(),
        P(("groups", "dp"), "tm", None, None, None),
    )
    out_specs = (
        P(("groups", "dp"), "tm", None, None, None),
        P(("groups", "dp"), "tm", None, None, None),
        P("groups", None, None, ("tm", "dp"), None),
    )
    order = ring_order(mesh, "tm")
    return jax.shard_map(functools.partial(shards, order), mesh=mesh, in_specs=in_specs, out_specs=out_specs, check_vma=False)
```

```python
import functools

import numpy as np

import jax
import jax.numpy as jnp
from jax import lax
from jax.sharding import PartitionSpec as P


def passed_along(value, axis, steps):
    count = lax.axis_size(axis)
    leading, last = (max(0, -steps), min(count, count - steps))
    return lax.ppermute(value, axis, [(source, source + steps) for source in range(leading, last)])


def swapped(value, axis):
    count = lax.axis_size(axis)
    return lax.ppermute(value, axis, [(source, count - 1 - source) for source in range(count)])


def ring_order(mesh, axis):
    devices = np.asarray(mesh.devices)
    at = mesh.axis_names.index(axis)
    count = devices.shape[at]
    line = [devices[tuple(i if d == at else 0 for d in range(devices.ndim))] for i in range(count)]
    try:
        coords = [tuple(d.coords) for d in line]
    except AttributeError:
        return list(range(count))

    def near(a, b):
        return sum(abs(x - y) for x, y in zip(coords[a], coords[b])) == 1

    best = [None]
    budget = [20000]

    def walk(path, seen):
        budget[0] -= 1
        if budget[0] < 0:
            return True
        if len(path) == count:
            if near(path[-1], path[0]):
                best[0] = list(path)
                return True
            if best[0] is None:
                best[0] = list(path)
            return False
        for nxt in range(count):
            if nxt not in seen and near(path[-1], nxt):
                path.append(nxt)
                seen.add(nxt)
                if walk(path, seen):
                    return True
                path.pop()
                seen.discard(nxt)
        return False

    walk([0], {0})
    return best[0] if best[0] is not None else list(range(count))


def ring_reduce_scatter(terms, axis, order, direction):
    count = len(order)
    place = [0] * count
    for position, owner in enumerate(order):
        place[owner] = position
    me = jnp.asarray(place, jnp.int32)[lax.axis_index(axis)]
    owners = jnp.asarray(order, jnp.int32)
    pairs = [(order[q], order[(q + direction) % count]) for q in range(count)]

    def own(step):
        chunk = (me - direction * (step + 1) + 2 * count) % count
        return lax.dynamic_index_in_dim(terms, owners[chunk], axis=1, keepdims=False)

    total = own(0)
    for step in range(count - 1):
        total = lax.ppermute(total, axis, pairs) + own(step + 1)
    return total


def convolve(source, kernel, time_pad, flipped):
    if flipped:
        kernel = lax.rev(kernel, (0, 1, 2))
        layout = "DHWOI"
    else:
        layout = "DHWIO"
    return lax.conv_general_dilated(
        source,
        kernel,
        (1, 1, 1),
        [time_pad, (1, 1), (1, 1)],
        dimension_numbers=("NDHWC", layout, "NDHWC"),
        preferred_element_type=jnp.float32,
    )


def kernel_terms(extended, own, cotangent):
    frames = cotangent.shape[1]
    height = cotangent.shape[2]
    width = cotangent.shape[3]
    chans = cotangent.shape[4]
    spaced = jnp.pad(extended, ((0, 0), (0, 0), (1, 1), (1, 1), (0, 0)))
    spaced_own = jnp.pad(own, ((0, 0), (0, 0), (1, 1), (1, 1), (0, 0)))
    flat_grad = cotangent.reshape(-1, chans)
    pieces = {}
    for kt in (2, 1, 0):
        for kh in range(3):
            for kw in range(3):
                if kt == 2:
                    window = spaced_own[:, :, kh : kh + height, kw : kw + width, :]
                else:
                    window = spaced[:, kt : kt + frames, kh : kh + height, kw : kw + width, :]
                window = window.reshape(-1, chans)
                pieces[kt, kh, kw] = lax.dot_general(
                    window,
                    flat_grad,
                    (((0,), (0,)), ((), ())),
                    preferred_element_type=jnp.float32,
                )
    pieces = [pieces[kt, kh, kw] for kt in (2, 1, 0) for kh in range(3) for kw in range(3)]
    return jnp.stack(pieces).reshape(3, 3, 3, chans, chans)


def shards(order, clips, kernel, cotangent):
    frames = clips.shape[1]
    wide = clips.astype(jnp.float32)
    act = jax.nn.silu(wide).astype(jnp.bfloat16)
    earlier = passed_along(act, "tm", 1)
    extended = jnp.concatenate([earlier, act], axis=1)

    terms = kernel_terms(extended, act, cotangent)
    owners = lax.axis_size("tm")
    pair = lax.axis_size("dp")
    chans = terms.shape[-1]
    me = lax.axis_index("dp")
    terms = lax.optimization_barrier(terms)
    terms = terms.reshape((27, owners, pair, chans // (owners * pair), chans))
    mine = lax.dynamic_index_in_dim(terms, me, axis=2, keepdims=False)
    theirs = lax.dynamic_index_in_dim(terms, pair - 1 - me, axis=2, keepdims=False)
    arrived = swapped(theirs, "dp")

    conv = convolve(extended, kernel, (0, 0), False)
    output = (wide + conv).astype(jnp.bfloat16)
    padded_grad = jnp.pad(cotangent, ((0, 0), (2, 2), (0, 0), (0, 0), (0, 0)))
    partial_grad = convolve(padded_grad, kernel, (0, 0), True)
    arrived, outgoing = lax.optimization_barrier((arrived, partial_grad[:, :2].astype(jnp.bfloat16)))
    returned = passed_along(outgoing, "tm", -1).astype(jnp.float32)
    returned = jnp.pad(returned, ((0, 0), (0, frames - 2), (0, 0), (0, 0), (0, 0)))
    grad_act = partial_grad[:, 2:] + returned
    sig = jax.nn.sigmoid(wide)
    grad_input = (
        cotangent.astype(jnp.float32) + grad_act * sig * (1.0 + wide * (1.0 - sig))
    ).astype(jnp.bfloat16)

    terms = mine + arrived
    split = chans // 2
    forward = ring_reduce_scatter(terms[..., :split], "tm", order, 1)
    backward = ring_reduce_scatter(terms[..., split:], "tm", order, -1)
    grad_kernel = jnp.concatenate([forward, backward], axis=-1)
    grad_kernel = lax.rev(grad_kernel.reshape((3, 3, 3) + grad_kernel.shape[1:]), (0,))
    return (output, grad_input, grad_kernel)


def solution(mesh):
    in_specs = (
        P(("groups", "dp"), "tm", None, None, None),
        P(),
        P(("groups", "dp"), "tm", None, None, None),
    )
    out_specs = (
        P(("groups", "dp"), "tm", None, None, None),
        P(("groups", "dp"), "tm", None, None, None),
        P("groups", None, None, ("tm", "dp"), None),
    )
    order = ring_order(mesh, "tm")
    return jax.shard_map(functools.partial(shards, order), mesh=mesh, in_specs=in_specs, out_specs=out_specs, check_vma=False)
```

```python
import functools

import numpy as np

import jax
import jax.numpy as jnp
from jax import lax
from jax.sharding import PartitionSpec as P


def passed_along(value, axis, steps):
    count = lax.axis_size(axis)
    leading, last = (max(0, -steps), min(count, count - steps))
    return lax.ppermute(value, axis, [(source, source + steps) for source in range(leading, last)])


def swapped(value, axis):
    count = lax.axis_size(axis)
    return lax.ppermute(value, axis, [(source, count - 1 - source) for source in range(count)])


def ring_order(mesh, axis):
    devices = np.asarray(mesh.devices)
    at = mesh.axis_names.index(axis)
    count = devices.shape[at]
    line = [devices[tuple(i if d == at else 0 for d in range(devices.ndim))] for i in range(count)]
    try:
        coords = [tuple(d.coords) for d in line]
    except AttributeError:
        return list(range(count))

    def near(a, b):
        return sum(abs(x - y) for x, y in zip(coords[a], coords[b])) == 1

    best = [None]
    budget = [20000]

    def walk(path, seen):
        budget[0] -= 1
        if budget[0] < 0:
            return True
        if len(path) == count:
            if near(path[-1], path[0]):
                best[0] = list(path)
                return True
            if best[0] is None:
                best[0] = list(path)
            return False
        for nxt in range(count):
            if nxt not in seen and near(path[-1], nxt):
                path.append(nxt)
                seen.add(nxt)
                if walk(path, seen):
                    return True
                path.pop()
                seen.discard(nxt)
        return False

    walk([0], {0})
    return best[0] if best[0] is not None else list(range(count))


def ring_reduce_scatter(terms, axis, order, direction):
    count = len(order)
    place = [0] * count
    for position, owner in enumerate(order):
        place[owner] = position
    me = jnp.asarray(place, jnp.int32)[lax.axis_index(axis)]
    owners = jnp.asarray(order, jnp.int32)
    pairs = [(order[q], order[(q + direction) % count]) for q in range(count)]

    def own(step):
        chunk = (me - direction * (step + 1) + 2 * count) % count
        return lax.dynamic_index_in_dim(terms, owners[chunk], axis=0, keepdims=False)

    total = own(0)
    for step in range(count - 1):
        total = lax.ppermute(total, axis, pairs) + own(step + 1)
    return total


def convolve(source, kernel, time_pad, flipped):
    if flipped:
        kernel = lax.rev(kernel, (0, 1, 2))
        layout = "DHWOI"
    else:
        layout = "DHWIO"
    return lax.conv_general_dilated(
        source,
        kernel,
        (1, 1, 1),
        [time_pad, (1, 1), (1, 1)],
        dimension_numbers=("NDHWC", layout, "NDHWC"),
        preferred_element_type=jnp.float32,
    )


def kernel_terms(extended, own, cotangent):
    frames = cotangent.shape[1]
    height = cotangent.shape[2]
    width = cotangent.shape[3]
    chans = cotangent.shape[4]
    spaced = jnp.pad(extended, ((0, 0), (0, 0), (1, 1), (1, 1), (0, 0)))
    spaced_own = jnp.pad(own, ((0, 0), (0, 0), (1, 1), (1, 1), (0, 0)))
    flat_grad = cotangent.reshape(-1, chans)
    pieces = {}
    for kt in (2, 1, 0):
        for kh in range(3):
            for kw in range(3):
                if kt == 2:
                    window = spaced_own[:, :, kh : kh + height, kw : kw + width, :]
                else:
                    window = spaced[:, kt : kt + frames, kh : kh + height, kw : kw + width, :]
                window = window.reshape(-1, chans)
                pieces[kt, kh, kw] = lax.dot_general(
                    window,
                    flat_grad,
                    (((0,), (0,)), ((), ())),
                    preferred_element_type=jnp.float32,
                )
    pieces = [pieces[kt, kh, kw] for kt in (2, 1, 0) for kh in range(3) for kw in range(3)]
    return pieces


def shards(order, clips, kernel, cotangent):
    frames = clips.shape[1]
    wide = clips.astype(jnp.float32)
    act = jax.nn.silu(wide).astype(jnp.bfloat16)
    earlier = passed_along(act, "tm", 1)
    extended = jnp.concatenate([earlier, act], axis=1)

    pieces = kernel_terms(extended, act, cotangent)
    owners = lax.axis_size("tm")
    pair = lax.axis_size("dp")
    chans = pieces[0].shape[-1]
    me = lax.axis_index("dp")
    pieces = [
        jnp.swapaxes(piece.reshape(owners, pair, chans // (owners * pair), chans), 0, 1)
        for piece in lax.optimization_barrier(pieces)
    ]
    terms = lax.optimization_barrier(jnp.stack(pieces, axis=2))
    mine = lax.dynamic_index_in_dim(terms, me, axis=0, keepdims=False)
    theirs = lax.dynamic_index_in_dim(terms, pair - 1 - me, axis=0, keepdims=False)
    arrived = swapped(theirs, "dp")

    conv = convolve(extended, kernel, (0, 0), False)
    output = (wide + conv).astype(jnp.bfloat16)
    padded_grad = jnp.pad(cotangent, ((0, 0), (2, 2), (0, 0), (0, 0), (0, 0)))
    partial_grad = convolve(padded_grad, kernel, (0, 0), True)
    arrived, outgoing = lax.optimization_barrier((arrived, partial_grad[:, :2].astype(jnp.bfloat16)))
    returned = passed_along(outgoing, "tm", -1).astype(jnp.float32)
    returned = jnp.pad(returned, ((0, 0), (0, frames - 2), (0, 0), (0, 0), (0, 0)))
    grad_act = partial_grad[:, 2:] + returned
    sig = jax.nn.sigmoid(wide)
    grad_input = (
        cotangent.astype(jnp.float32) + grad_act * sig * (1.0 + wide * (1.0 - sig))
    ).astype(jnp.bfloat16)

    terms = mine + arrived
    split = (terms.shape[1] + 1) // 2
    forward = ring_reduce_scatter(terms[:, :split], "tm", order, 1)
    backward = ring_reduce_scatter(terms[:, split:], "tm", order, -1)
    grad_kernel = jnp.concatenate([forward, backward], axis=0)
    grad_kernel = lax.rev(grad_kernel.reshape((3, 3, 3) + grad_kernel.shape[1:]), (0,))
    return (output, grad_input, grad_kernel)


def solution(mesh):
    in_specs = (
        P(("groups", "dp"), "tm", None, None, None),
        P(),
        P(("groups", "dp"), "tm", None, None, None),
    )
    out_specs = (
        P(("groups", "dp"), "tm", None, None, None),
        P(("groups", "dp"), "tm", None, None, None),
        P("groups", None, None, ("tm", "dp"), None),
    )
    order = ring_order(mesh, "tm")
    return jax.shard_map(functools.partial(shards, order), mesh=mesh, in_specs=in_specs, out_specs=out_specs, check_vma=False)
```

```python
import jax
import jax.numpy as jnp
from jax import lax
from jax.sharding import PartitionSpec as P


def passed_along(value, axis, steps):
    count = lax.axis_size(axis)
    leading, last = (max(0, -steps), min(count, count - steps))
    return lax.ppermute(value, axis, [(source, source + steps) for source in range(leading, last)])


def convolve(source, kernel, time_pad, flipped):
    if flipped:
        kernel = lax.rev(kernel, (0, 1, 2))
        layout = "DHWOI"
    else:
        layout = "DHWIO"
    return lax.conv_general_dilated(
        source,
        kernel,
        (1, 1, 1),
        [time_pad, (1, 1), (1, 1)],
        dimension_numbers=("NDHWC", layout, "NDHWC"),
        preferred_element_type=jnp.float32,
    )


def kernel_terms(extended, own, cotangent):
    frames = cotangent.shape[1]
    height = cotangent.shape[2]
    width = cotangent.shape[3]
    chans = cotangent.shape[4]
    wide = width + 2
    span = height * wide

    def flat(value):
        spaced = jnp.pad(value, ((0, 0), (0, 0), (1, 1), (1, 1), (0, 0)))
        spaced = spaced.reshape(spaced.shape[:2] + ((height + 2) * wide, chans))
        return jnp.pad(spaced, ((0, 0), (0, 0), (0, 2), (0, 0)))

    spaced = flat(extended)
    spaced_own = flat(own)
    flat_grad = jnp.pad(cotangent, ((0, 0), (0, 0), (0, 0), (0, 2), (0, 0))).reshape(-1, chans)
    pieces = {}
    for kt in (2, 1, 0):
        for kh in range(3):
            for kw in range(3):
                start = kh * wide + kw
                if kt == 2:
                    window = spaced_own[:, :, start : start + span, :]
                else:
                    window = spaced[:, kt : kt + frames, start : start + span, :]
                window = window.reshape(-1, chans)
                pieces[kt, kh, kw] = lax.dot_general(
                    window,
                    flat_grad,
                    (((0,), (0,)), ((), ())),
                    preferred_element_type=jnp.float32,
                )
    pieces = [pieces[kt, kh, kw] for kt in (2, 1, 0) for kh in range(3) for kw in range(3)]
    return jnp.stack(pieces).reshape(3, 3, 3, chans, chans)


def shards(clips, kernel, cotangent):
    frames = clips.shape[1]
    wide = clips.astype(jnp.float32)
    act = jax.nn.silu(wide).astype(jnp.bfloat16)
    earlier = passed_along(act, "tm", 1)
    extended = jnp.concatenate([earlier, act], axis=1)
    conv = convolve(extended, kernel, (0, 0), False)
    output = (wide + conv).astype(jnp.bfloat16)
    padded_grad = jnp.pad(cotangent, ((0, 0), (2, 2), (0, 0), (0, 0), (0, 0)))
    partial_grad = convolve(padded_grad, kernel, (0, 0), True)
    returned = passed_along(partial_grad[:, :2].astype(jnp.bfloat16), "tm", -1).astype(jnp.float32)
    returned = jnp.pad(returned, ((0, 0), (0, frames - 2), (0, 0), (0, 0), (0, 0)))
    grad_act = partial_grad[:, 2:] + returned
    sig = jax.nn.sigmoid(wide)
    grad_input = (
        cotangent.astype(jnp.float32) + grad_act * sig * (1.0 + wide * (1.0 - sig))
    ).astype(jnp.bfloat16)
    terms = kernel_terms(extended, act, cotangent)
    grad_kernel = lax.rev(lax.psum_scatter(terms, ("tm", "dp"), scatter_dimension=3, tiled=True), (0,))
    return (output, grad_input, grad_kernel)


def solution(mesh):
    in_specs = (
        P(("groups", "dp"), "tm", None, None, None),
        P(),
        P(("groups", "dp"), "tm", None, None, None),
    )
    out_specs = (
        P(("groups", "dp"), "tm", None, None, None),
        P(("groups", "dp"), "tm", None, None, None),
        P("groups", None, None, ("tm", "dp"), None),
    )
    return jax.shard_map(shards, mesh=mesh, in_specs=in_specs, out_specs=out_specs, check_vma=False)
```

```python
import jax
import jax.numpy as jnp
from jax import lax
from jax.sharding import PartitionSpec as P


def passed_along(value, axis, steps):
    count = lax.axis_size(axis)
    leading, last = (max(0, -steps), min(count, count - steps))
    return lax.ppermute(value, axis, [(source, source + steps) for source in range(leading, last)])


def convolve(source, kernel, time_pad, flipped):
    if flipped:
        kernel = lax.rev(kernel, (0, 1, 2))
        layout = "DHWOI"
    else:
        layout = "DHWIO"
    return lax.conv_general_dilated(
        source,
        kernel,
        (1, 1, 1),
        [time_pad, (1, 1), (1, 1)],
        dimension_numbers=("NDHWC", layout, "NDHWC"),
        preferred_element_type=jnp.float32,
    )


def kernel_terms(extended, own, cotangent):
    frames = cotangent.shape[1]
    height = cotangent.shape[2]
    width = cotangent.shape[3]
    chans = cotangent.shape[4]
    spaced = jnp.pad(extended, ((0, 0), (0, 0), (1, 1), (1, 1), (0, 0)))
    spaced_own = jnp.pad(own, ((0, 0), (0, 0), (1, 1), (1, 1), (0, 0)))
    flat_grad = cotangent.reshape(-1, chans)
    padded_grad = jnp.pad(cotangent, ((0, 0), (1, 1), (0, 0), (0, 0), (0, 0)))
    shifted_grad = jnp.concatenate(
        [padded_grad[:, 1 - kt : 2 - kt + frames] for kt in range(2)], axis=-1
    ).reshape(-1, 2 * chans)
    pieces = {}
    for kh in range(3):
        for kw in range(3):
            window = spaced_own[:, :, kh : kh + height, kw : kw + width, :].reshape(-1, chans)
            pieces[2, kh, kw] = lax.dot_general(
                window, flat_grad, (((0,), (0,)), ((), ())), preferred_element_type=jnp.float32
            )
    for kh in range(3):
        for kw in range(3):
            window = spaced[:, : frames + 1, kh : kh + height, kw : kw + width, :].reshape(-1, chans)
            both = lax.dot_general(
                window, shifted_grad, (((0,), (0,)), ((), ())), preferred_element_type=jnp.float32
            )
            pieces[0, kh, kw] = both[:, :chans]
            pieces[1, kh, kw] = both[:, chans:]
    pieces = [pieces[kt, kh, kw] for kt in (2, 1, 0) for kh in range(3) for kw in range(3)]
    return jnp.stack(pieces).reshape(3, 3, 3, chans, chans)


def shards(clips, kernel, cotangent):
    frames = clips.shape[1]
    wide = clips.astype(jnp.float32)
    act = jax.nn.silu(wide).astype(jnp.bfloat16)
    earlier = passed_along(act, "tm", 1)
    extended = jnp.concatenate([earlier, act], axis=1)
    conv = convolve(extended, kernel, (0, 0), False)
    output = (wide + conv).astype(jnp.bfloat16)
    padded_grad = jnp.pad(cotangent, ((0, 0), (2, 2), (0, 0), (0, 0), (0, 0)))
    partial_grad = convolve(padded_grad, kernel, (0, 0), True)
    returned = passed_along(partial_grad[:, :2].astype(jnp.bfloat16), "tm", -1).astype(jnp.float32)
    returned = jnp.pad(returned, ((0, 0), (0, frames - 2), (0, 0), (0, 0), (0, 0)))
    grad_act = partial_grad[:, 2:] + returned
    sig = jax.nn.sigmoid(wide)
    grad_input = (
        cotangent.astype(jnp.float32) + grad_act * sig * (1.0 + wide * (1.0 - sig))
    ).astype(jnp.bfloat16)
    terms = kernel_terms(extended, act, cotangent)
    grad_kernel = lax.rev(lax.psum_scatter(terms, ("tm", "dp"), scatter_dimension=3, tiled=True), (0,))
    return (output, grad_input, grad_kernel)


def solution(mesh):
    in_specs = (
        P(("groups", "dp"), "tm", None, None, None),
        P(),
        P(("groups", "dp"), "tm", None, None, None),
    )
    out_specs = (
        P(("groups", "dp"), "tm", None, None, None),
        P(("groups", "dp"), "tm", None, None, None),
        P("groups", None, None, ("tm", "dp"), None),
    )
    return jax.shard_map(shards, mesh=mesh, in_specs=in_specs, out_specs=out_specs, check_vma=False)
```

```python
import jax
import jax.numpy as jnp
from jax import lax
from jax.sharding import PartitionSpec as P


def passed_along(value, axis, steps):
    count = lax.axis_size(axis)
    leading, last = (max(0, -steps), min(count, count - steps))
    return lax.ppermute(value, axis, [(source, source + steps) for source in range(leading, last)])


def convolve(source, kernel, time_pad, flipped):
    if flipped:
        kernel = lax.rev(kernel, (0, 1, 2))
        layout = "DHWOI"
    else:
        layout = "DHWIO"
    return lax.conv_general_dilated(
        source,
        kernel,
        (1, 1, 1),
        [time_pad, (1, 1), (1, 1)],
        dimension_numbers=("NDHWC", layout, "NDHWC"),
        preferred_element_type=jnp.float32,
    )


def kernel_terms(extended, own, cotangent):
    frames = cotangent.shape[1]
    height = cotangent.shape[2]
    width = cotangent.shape[3]
    chans = cotangent.shape[4]
    spaced = jnp.pad(extended, ((0, 0), (0, 0), (1, 1), (1, 1), (0, 0)))
    spaced_own = jnp.pad(own, ((0, 0), (0, 0), (1, 1), (1, 1), (0, 0)))
    flat_grad = cotangent.reshape(-1, chans)
    padded_grad = jnp.pad(cotangent, ((0, 0), (1, 1), (0, 0), (0, 0), (0, 0)))
    shifted_grad = jnp.concatenate(
        [padded_grad[:, 1 - kt : 2 - kt + frames] for kt in range(2)], axis=-1
    ).reshape(-1, 2 * chans)
    pieces = {}
    for kh in range(3):
        for kw in range(3):
            window = spaced_own[:, :, kh : kh + height, kw : kw + width, :].reshape(-1, chans)
            pieces[2, kh, kw] = lax.dot_general(
                window, flat_grad, (((0,), (0,)), ((), ())), preferred_element_type=jnp.float32
            )
    for kh in range(3):
        for kw in range(3):
            window = spaced[:, : frames + 1, kh : kh + height, kw : kw + width, :].reshape(-1, chans)
            both = lax.dot_general(
                window, shifted_grad, (((0,), (0,)), ((), ())), preferred_element_type=jnp.float32
            )
            pieces[kh, kw] = jnp.concatenate([both, pieces[2, kh, kw]], axis=-1)
    rows = [pieces[kh, kw] for kh in range(3) for kw in range(3)]
    return jnp.stack(rows).reshape(3, 3, chans, 3, chans)


def shards(clips, kernel, cotangent):
    frames = clips.shape[1]
    wide = clips.astype(jnp.float32)
    act = jax.nn.silu(wide).astype(jnp.bfloat16)
    earlier = passed_along(act, "tm", 1)
    extended = jnp.concatenate([earlier, act], axis=1)
    conv = convolve(extended, kernel, (0, 0), False)
    output = (wide + conv).astype(jnp.bfloat16)
    padded_grad = jnp.pad(cotangent, ((0, 0), (2, 2), (0, 0), (0, 0), (0, 0)))
    partial_grad = convolve(padded_grad, kernel, (0, 0), True)
    returned = passed_along(partial_grad[:, :2].astype(jnp.bfloat16), "tm", -1).astype(jnp.float32)
    returned = jnp.pad(returned, ((0, 0), (0, frames - 2), (0, 0), (0, 0), (0, 0)))
    grad_act = partial_grad[:, 2:] + returned
    sig = jax.nn.sigmoid(wide)
    grad_input = (
        cotangent.astype(jnp.float32) + grad_act * sig * (1.0 + wide * (1.0 - sig))
    ).astype(jnp.bfloat16)
    terms = kernel_terms(extended, act, cotangent)
    grad_kernel = lax.psum_scatter(terms, ("tm", "dp"), scatter_dimension=2, tiled=True)
    grad_kernel = jnp.transpose(grad_kernel, (3, 0, 1, 2, 4))
    return (output, grad_input, grad_kernel)


def solution(mesh):
    in_specs = (
        P(("groups", "dp"), "tm", None, None, None),
        P(),
        P(("groups", "dp"), "tm", None, None, None),
    )
    out_specs = (
        P(("groups", "dp"), "tm", None, None, None),
        P(("groups", "dp"), "tm", None, None, None),
        P("groups", None, None, ("tm", "dp"), None),
    )
    return jax.shard_map(shards, mesh=mesh, in_specs=in_specs, out_specs=out_specs, check_vma=False)
```

```python
import jax
import jax.numpy as jnp
from jax import lax
from jax.sharding import PartitionSpec as P


def passed_along(value, axis, steps):
    count = lax.axis_size(axis)
    leading, last = (max(0, -steps), min(count, count - steps))
    return lax.ppermute(value, axis, [(source, source + steps) for source in range(leading, last)])


def convolve(source, kernel, time_pad, flipped):
    if flipped:
        kernel = lax.rev(kernel, (0, 1, 2))
        layout = "DHWOI"
    else:
        layout = "DHWIO"
    return lax.conv_general_dilated(
        source,
        kernel,
        (1, 1, 1),
        [time_pad, (1, 1), (1, 1)],
        dimension_numbers=("NDHWC", layout, "NDHWC"),
        preferred_element_type=jnp.float32,
    )


def kernel_terms(extended, own, cotangent):
    frames = cotangent.shape[1]
    height = cotangent.shape[2]
    width = cotangent.shape[3]
    chans = cotangent.shape[4]
    spaced = jnp.pad(extended, ((0, 0), (0, 0), (1, 1), (1, 1), (0, 0)))
    spaced_own = jnp.pad(own, ((0, 0), (0, 0), (1, 1), (1, 1), (0, 0)))
    flat_grad = cotangent.reshape(-1, chans)
    padded_grad = jnp.pad(cotangent, ((0, 0), (1, 1), (0, 0), (0, 0), (0, 0)))
    shifted_grad = jnp.concatenate(
        [padded_grad[:, 1 - kt : 2 - kt + frames] for kt in range(2)], axis=-1
    ).reshape(-1, 2 * chans)
    pieces = {}
    for kh in range(3):
        for kw in range(3):
            window = spaced_own[:, :, kh : kh + height, kw : kw + width, :].reshape(-1, chans)
            pieces[2, kh, kw] = lax.dot_general(
                window, flat_grad, (((0,), (0,)), ((), ())), preferred_element_type=jnp.float32
            )
    for kh in range(3):
        for kw in range(3):
            window = spaced[:, : frames + 1, kh : kh + height, kw : kw + width, :].reshape(-1, chans)
            both = lax.dot_general(
                shifted_grad.reshape(-1, 2, chans),
                window,
                (((0,), (0,)), ((), ())),
                preferred_element_type=jnp.float32,
            )
            pieces[0, kh, kw] = both[0].T
            pieces[1, kh, kw] = both[1].T
    pieces = [pieces[kt, kh, kw] for kt in (2, 1, 0) for kh in range(3) for kw in range(3)]
    return jnp.stack(pieces).reshape(3, 3, 3, chans, chans)


def shards(clips, kernel, cotangent):
    frames = clips.shape[1]
    wide = clips.astype(jnp.float32)
    act = jax.nn.silu(wide).astype(jnp.bfloat16)
    earlier = passed_along(act, "tm", 1)
    extended = jnp.concatenate([earlier, act], axis=1)
    conv = convolve(extended, kernel, (0, 0), False)
    output = (wide + conv).astype(jnp.bfloat16)
    padded_grad = jnp.pad(cotangent, ((0, 0), (2, 2), (0, 0), (0, 0), (0, 0)))
    partial_grad = convolve(padded_grad, kernel, (0, 0), True)
    returned = passed_along(partial_grad[:, :2].astype(jnp.bfloat16), "tm", -1).astype(jnp.float32)
    returned = jnp.pad(returned, ((0, 0), (0, frames - 2), (0, 0), (0, 0), (0, 0)))
    grad_act = partial_grad[:, 2:] + returned
    sig = jax.nn.sigmoid(wide)
    grad_input = (
        cotangent.astype(jnp.float32) + grad_act * sig * (1.0 + wide * (1.0 - sig))
    ).astype(jnp.bfloat16)
    terms = kernel_terms(extended, act, cotangent)
    grad_kernel = lax.rev(lax.psum_scatter(terms, ("tm", "dp"), scatter_dimension=3, tiled=True), (0,))
    return (output, grad_input, grad_kernel)


def solution(mesh):
    in_specs = (
        P(("groups", "dp"), "tm", None, None, None),
        P(),
        P(("groups", "dp"), "tm", None, None, None),
    )
    out_specs = (
        P(("groups", "dp"), "tm", None, None, None),
        P(("groups", "dp"), "tm", None, None, None),
        P("groups", None, None, ("tm", "dp"), None),
    )
    return jax.shard_map(shards, mesh=mesh, in_specs=in_specs, out_specs=out_specs, check_vma=False)
```
